128 devices in a mesh: seq: 16 (over z, x_lo, core), chan: 4 (over y), rep: 2 (over x_hi).
Axes of the slice: x: 4 (x_hi: 2, x_lo: 2; x = x_hi * 2 + x_lo), y: 4, z: 4, core: 2. Of those that a mesh axis runs over, the one named last changes fastest.
Arguments:
- inputs: bfloat16 [2, 4096, 2048], P('rep', 'seq', 'chan'), may hold values from -6 to 6
- w_in: bfloat16 [2048, 1536], P('chan'), may hold values from -0.25 to 0.25
- w_out: bfloat16 [2048, 2048], P('chan'), may hold values from -0.125 to 0.125
- filt_fwd: float32 [4096, 2048], P('seq', 'chan'), may hold values from -0.09375 to 0.09375
- filt_bwd: float32 [4096, 2048], P('seq', 'chan'), may hold values from -0.09375 to 0.09375
- skip_gain: float32 [2048], P('chan'), may hold values from -4 to 4
- cotangent: bfloat16 [2, 4096, 2048], P('rep', 'seq', 'chan'), may hold values from -6 to 6
Outputs:
- layer_out: bfloat16 [2, 4096, 2048], P('rep', 'seq', 'chan')
- d_input: bfloat16 [2, 4096, 2048], P('rep', 'seq', 'chan')
- d_w_in: float32 [2048, 1536], P('chan')
- d_w_out: float32 [2048, 2048], P('chan')
- d_filt_fwd: float32 [4096, 2048], P('seq', 'chan')
- d_filt_bwd: float32 [4096, 2048], P('seq', 'chan')
- d_skip: float32 [2048], P('chan')
The draws below stay inside these ranges and needn't reach their ends.
All inputs are finite; a program needn't handle non-finite values.
Results may differ from the reference program's by a relative error of at most 0.005.
Values may be sent and summed in bfloat16 or wider, within the bound.
No kernel may reach another device: no remote copies, remote signals or barrier semaphores. Data moves between devices by JAX's collectives and lax.ppermute only.
A program may use at most 128 MiB of HBM per device.

```python
import math
import jax
import jax.numpy as jnp
from jax import lax

D = 2048
BLOCK = 512
L = 4096
REPS = 2


def shard_levels(rng, extent, pieces, low, high):
    factor_of, own = 1.0, jax.random.fold_in(rng, 6)
    for axis_at, blocks in pieces:
        draws = jnp.exp(jax.random.uniform(jax.random.fold_in(own, axis_at), (blocks,), jnp.float32, low / len(pieces), high / len(pieces)))
        factor_of = factor_of * jnp.repeat(draws, extent[axis_at] // blocks).reshape([-1 if axis == axis_at else 1 for axis in range(len(extent))])
    return factor_of


def bell_draw(stream_key, dims, deviation, most, pieces=(), held_as=jnp.bfloat16):
    entries = deviation * jax.random.normal(stream_key, dims, jnp.float32)
    if pieces:
        entries = entries * shard_levels(stream_key, dims, pieces, -0.22, 0.18)
    return jnp.clip(entries, -most, most).astype(held_as)


def setup_inputs(seed: int = 0) -> dict:
    streams_of = jax.random.split(jax.random.key(seed), 8)
    return {
        "inputs": bell_draw(streams_of[0], (REPS, L, D), 1.0, 6.0, ((0, 2), (1, 16), (2, 4))),
        "w_in": bell_draw(streams_of[1], (D, 3 * BLOCK), BLOCK ** -0.5, 0.25, ((0, 4),)),
        "w_out": bell_draw(streams_of[2], (D, D), D ** -0.5, 0.125, ((0, 4),)),
        "filt_fwd": bell_draw(streams_of[3], (L, D), L ** -0.5, 0.09375, ((0, 16), (1, 4)), jnp.float32),
        "filt_bwd": bell_draw(streams_of[4], (L, D), L ** -0.5, 0.09375, ((0, 16), (1, 4)), jnp.float32),
        "skip_gain": bell_draw(streams_of[5], (D,), 1.0, 4.0, ((0, 4),), jnp.float32),
        "cotangent": bell_draw(streams_of[6], (REPS, L, D), 1.0, 6.0, ((0, 2), (1, 16), (2, 4))),
    }


def one_replica(input_rep, grad_rep, w_blocks, w_out, gain_fwd, gain_bwd, skip_gain):
    block_count = D // BLOCK
    input_blocks = input_rep.reshape(L, block_count, BLOCK).astype(jnp.float32)
    projected = jnp.einsum('mni,nisj->smnj', input_blocks, w_blocks).reshape(3, L, D)
    keys, values, queries = (projected[0], projected[1], projected[2])
    mixed = keys * values
    mixed_spec = jnp.fft.fft(mixed, axis=0)
    conv_out = jnp.real(jnp.fft.ifft(gain_fwd * mixed_spec, axis=0)).astype(jnp.float32) + skip_gain * mixed
    gated = (queries * conv_out).astype(jnp.bfloat16)
    layer_out = jnp.dot(gated, w_out, preferred_element_type=jnp.float32).astype(jnp.bfloat16)
    grad_gated = jnp.dot(grad_rep, w_out.T, preferred_element_type=jnp.float32)
    grad_wout = jnp.dot(gated.T, grad_rep, preferred_element_type=jnp.float32)
    grad_queries = grad_gated * conv_out
    grad_conv = grad_gated * queries
    grad_spec = jnp.fft.fft(grad_conv, axis=0)
    back = jnp.real(jnp.fft.ifft(gain_bwd * grad_spec, axis=0)).astype(jnp.float32)
    grad_hfwd = jnp.real(jnp.fft.ifft(grad_spec * jnp.conj(mixed_spec), axis=0)).astype(jnp.float32)
    grad_hbwd = jnp.real(jnp.fft.ifft(jnp.conj(grad_spec) * mixed_spec, axis=0)).astype(jnp.float32)
    grad_mixed = back + skip_gain * grad_conv
    grad_pre = jnp.stack([grad_mixed * values, grad_mixed * keys, grad_queries]).astype(jnp.bfloat16)
    pre_blocks = grad_pre.reshape(3, L, block_count, BLOCK).astype(jnp.float32)
    d_input = jnp.einsum('smnj,nisj->mni', pre_blocks, w_blocks).reshape(L, D).astype(jnp.bfloat16)
    grad_win = jnp.einsum('mni,smnj->nisj', input_blocks, pre_blocks).reshape(D, 3 * BLOCK)
    grad_skip = lax.optimization_barrier(jnp.sum(grad_conv * mixed, axis=0))
    return (layer_out, d_input, grad_win, grad_wout, grad_hfwd, grad_hbwd, grad_skip)

def reference(inputs, w_in, w_out, filt_fwd, filt_bwd, skip_gain, cotangent):
    block_count = D // BLOCK
    w_blocks = w_in.reshape(block_count, BLOCK, 3, BLOCK).astype(jnp.float32)
    spec_fwd = jnp.fft.fft(filt_fwd, axis=0)
    spec_bwd = jnp.fft.fft(filt_bwd, axis=0)
    gain_fwd = spec_fwd + jnp.conj(spec_bwd)
    gain_bwd = jnp.conj(spec_fwd) + spec_bwd
    outs_list = []
    inputs_list = []
    total_win = jnp.zeros((D, 3 * BLOCK), jnp.float32)
    total_wout = jnp.zeros((D, D), jnp.float32)
    total_hfwd = jnp.zeros((L, D), jnp.float32)
    total_hbwd = jnp.zeros((L, D), jnp.float32)
    total_skip = jnp.zeros((D,), jnp.float32)
    for replica in range(REPS):
        results = one_replica(inputs[replica], cotangent[replica], w_blocks, w_out, gain_fwd, gain_bwd, skip_gain)
        outs_list.append(results[0])
        inputs_list.append(results[1])
        total_win = total_win + results[2]
        total_wout = total_wout + results[3]
        total_hfwd = total_hfwd + results[4]
        total_hbwd = total_hbwd + results[5]
        total_skip = total_skip + results[6]
    scale = 1.0 / math.sqrt(REPS * L)
    return (jnp.stack(outs_list), jnp.stack(inputs_list), total_win * scale, total_wout * scale, total_hfwd * scale, total_hbwd * scale, total_skip * scale)
```

```python
import math

import jax
import jax.numpy as jnp
import numpy as np
from jax import lax
from jax.sharding import PartitionSpec as P

BLOCK = 512

HIGHEST_PRECISION = lax.Precision.HIGHEST


def factor_split(length):
    first = 1 << (int(math.log2(length)) // 2)
    return first, length // first


def unit_table(size):
    index_row = np.arange(size)
    angle = 2.0 * np.pi * ((index_row[:, None] * index_row[None, :]) % size) / size
    return (jnp.asarray(np.cos(angle), jnp.float32), jnp.asarray(np.sin(angle), jnp.float32))


def twiddle_table(rows, cols):
    length = rows * cols
    phase = (np.arange(rows)[:, None] * np.arange(cols)[None, :]) % length
    angle = 2.0 * np.pi * phase / length
    return (jnp.asarray(np.cos(angle), jnp.float32), jnp.asarray(np.sin(angle), jnp.float32))


def table_apply(table, fields, form):
    return jnp.einsum(form, table, fields, precision=HIGHEST_PRECISION)


def real_spectrum(signal):
    field_count, length, width = signal.shape
    first, second = factor_split(length)
    grid = signal.reshape(field_count, first, second, width)
    cos_a, sin_a = unit_table(first)
    cos_b, sin_b = unit_table(second)
    cos_t, sin_t = twiddle_table(first, second)
    y_re = table_apply(cos_a, grid, "kn,fnmc->fkmc")
    y_im = -table_apply(sin_a, grid, "kn,fnmc->fkmc")
    cos_t = cos_t[None, :, :, None]
    sin_t = sin_t[None, :, :, None]
    z_re = y_re * cos_t + y_im * sin_t
    z_im = y_im * cos_t - y_re * sin_t
    x_re = table_apply(cos_b, z_re, "jm,fkmc->fjkc") + table_apply(sin_b, z_im, "jm,fkmc->fjkc")
    x_im = table_apply(cos_b, z_im, "jm,fkmc->fjkc") - table_apply(sin_b, z_re, "jm,fkmc->fjkc")
    return x_re, x_im


def real_inverse(spec_re, spec_im):
    field_count, second, first, width = spec_re.shape
    length = first * second
    cos_a, sin_a = unit_table(first)
    cos_b, sin_b = unit_table(second)
    cos_t, sin_t = twiddle_table(first, second)
    a_re = table_apply(cos_b, spec_re, "mj,fjkc->fmkc") - table_apply(sin_b, spec_im, "mj,fjkc->fmkc")
    a_im = table_apply(cos_b, spec_im, "mj,fjkc->fmkc") + table_apply(sin_b, spec_re, "mj,fjkc->fmkc")
    cos_t = cos_t.T[None, :, :, None]
    sin_t = sin_t.T[None, :, :, None]
    b_re = a_re * cos_t - a_im * sin_t
    b_im = a_re * sin_t + a_im * cos_t
    out = table_apply(cos_a, b_re, "nk,fmkc->fnmc") - table_apply(sin_a, b_im, "nk,fmkc->fnmc")
    return out.reshape(field_count, length, width) * (1.0 / length)


def lag_reverse(signal, axis):
    return jnp.roll(jnp.flip(signal, axis=axis), 1, axis=axis)


def complex_product(left_re, left_im, right_re, right_im):
    return (left_re * right_re - left_im * right_im, left_re * right_im + left_im * right_re)


def to_channels(fields):
    return lax.all_to_all(fields, "seq", split_axis=2, concat_axis=1, tiled=True)


def to_rows(fields):
    return lax.all_to_all(fields, "seq", split_axis=1, concat_axis=2, tiled=True)


def on_device(inputs, w_in, w_out, filt_fwd, filt_bwd, skip_gain, cotangent):
    input_rows = inputs[0]
    row_count, chan_width = input_rows.shape
    block_count = chan_width // BLOCK
    input_blocks = input_rows.reshape(row_count, block_count, BLOCK)
    w_blocks = w_in.reshape(block_count, BLOCK, 3, BLOCK)
    grad_rows = cotangent[0]
    piece = lax.all_gather(grad_rows, "chan", axis=1, tiled=True)
    projected = jnp.einsum(
        "mni,nisj->smnj", input_blocks, w_blocks, preferred_element_type=jnp.float32
    )
    projected = projected.reshape(3, row_count, chan_width)
    keys, values, queries = (projected[0], projected[1], projected[2])
    mixed = keys * values
    spread = to_channels(jnp.stack([mixed, filt_fwd, filt_bwd]))
    mixed_cs = spread[0]
    joint_filter = spread[1] + lag_reverse(spread[2], 0)
    spec_re, spec_im = real_spectrum(jnp.stack([mixed_cs, joint_filter]))
    mix_re, mix_im = (spec_re[0], spec_im[0])
    gain_re, gain_im = (spec_re[1], spec_im[1])
    joint_re, joint_im = complex_product(gain_re, gain_im, mix_re, mix_im)
    long_conv = to_rows(real_inverse(joint_re[None], joint_im[None]))[0]
    conv_out = long_conv + skip_gain * mixed
    gated = (queries * conv_out).astype(jnp.bfloat16)
    out_terms = jnp.dot(gated, w_out, preferred_element_type=jnp.float32)
    layer_out = lax.psum_scatter(out_terms, "chan", scatter_dimension=1, tiled=True).astype(
        jnp.bfloat16
    )
    grad_gated = lax.dot_general(
        piece, w_out, (((1,), (1,)), ((), ())), preferred_element_type=jnp.float32
    )
    grad_wout = lax.dot_general(
        gated, piece, (((0,), (0,)), ((), ())), preferred_element_type=jnp.float32
    )
    grad_wout = lax.psum(grad_wout, ("seq", "rep"))
    grad_queries = grad_gated * conv_out
    grad_conv = grad_gated * queries
    grad_cs = to_channels(grad_conv[None])
    grad_re, grad_im = real_spectrum(grad_cs)
    grad_re, grad_im = (grad_re[0], grad_im[0])
    back_re, back_im = complex_product(gain_re, -gain_im, grad_re, grad_im)
    cross_re, cross_im = complex_product(grad_re, grad_im, mix_re, -mix_im)
    results = real_inverse(jnp.stack([back_re, cross_re]), jnp.stack([back_im, cross_im]))
    back = to_rows(results[0][None])[0]
    grad_hfwd = lax.psum(results[1], "rep")
    grad_hbwd = lag_reverse(grad_hfwd, 0)
    filt_grads = to_rows(jnp.stack([grad_hfwd, grad_hbwd]))
    grad_mixed = back + skip_gain * grad_conv
    grad_pre = jnp.stack([grad_mixed * values, grad_mixed * keys, grad_queries]).astype(
        jnp.bfloat16
    )
    pre_blocks = grad_pre.reshape(3, row_count, block_count, BLOCK)
    d_input = jnp.einsum("smnj,nisj->mni", pre_blocks, w_blocks, preferred_element_type=jnp.float32)
    d_input = d_input.reshape(row_count, chan_width).astype(jnp.bfloat16)
    grad_win = jnp.einsum(
        "mni,smnj->nisj", input_blocks, pre_blocks, preferred_element_type=jnp.float32
    )
    grad_win = grad_win.reshape(chan_width, 3 * BLOCK)
    grad_skip = jnp.sum(grad_conv * mixed, axis=0)
    grad_win, grad_skip = lax.psum((grad_win, grad_skip), ("seq", "rep"))
    scale = 1.0 / math.sqrt(lax.axis_size("rep") * lax.axis_size("seq") * row_count)
    return (
        layer_out[None],
        d_input[None],
        grad_win * scale,
        grad_wout * scale,
        filt_grads[0] * scale,
        filt_grads[1] * scale,
        grad_skip * scale,
    )


def solution(mesh):
    return jax.shard_map(
        on_device,
        mesh=mesh,
        in_specs=(
            P("rep", "seq", "chan"),
            P("chan", None),
            P("chan", None),
            P("seq", "chan"),
            P("seq", "chan"),
            P("chan"),
            P("rep", "seq", "chan"),
        ),
        out_specs=(
            P("rep", "seq", "chan"),
            P("rep", "seq", "chan"),
            P("chan", None),
            P("chan", None),
            P("seq", "chan"),
            P("seq", "chan"),
            P("chan"),
        ),
        check_vma=False,
    )
```

```python
import math

import jax
import jax.numpy as jnp
import numpy as np
from jax import lax
from jax.sharding import PartitionSpec as P

BLOCK = 512

HIGHEST_PRECISION = lax.Precision.HIGHEST


def factor_split(length):
    second = 256
    return length // second, second


def unit_table(size):
    index_row = np.arange(size)
    angle = 2.0 * np.pi * ((index_row[:, None] * index_row[None, :]) % size) / size
    return (jnp.asarray(np.cos(angle), jnp.float32), jnp.asarray(np.sin(angle), jnp.float32))


def twiddle_table(rows, cols):
    length = rows * cols
    phase = (np.arange(rows)[:, None] * np.arange(cols)[None, :]) % length
    angle = 2.0 * np.pi * phase / length
    return (jnp.asarray(np.cos(angle), jnp.float32), jnp.asarray(np.sin(angle), jnp.float32))


def table_apply(table, fields, form):
    return jnp.einsum(form, table, fields, precision=HIGHEST_PRECISION)


def real_spectrum(signal):
    field_count, width, length = signal.shape
    first, second = factor_split(length)
    grid = signal.reshape(field_count, width, first, second)
    cos_a, sin_a = unit_table(first)
    cos_b, sin_b = unit_table(second)
    cos_t, sin_t = twiddle_table(first, second)
    y_re = table_apply(cos_a, grid, "kn,fcnm->fckm")
    y_im = -table_apply(sin_a, grid, "kn,fcnm->fckm")
    z_re = y_re * cos_t + y_im * sin_t
    z_im = y_im * cos_t - y_re * sin_t
    x_re = table_apply(cos_b, z_re, "jm,fckm->fckj") + table_apply(sin_b, z_im, "jm,fckm->fckj")
    x_im = table_apply(cos_b, z_im, "jm,fckm->fckj") - table_apply(sin_b, z_re, "jm,fckm->fckj")
    return x_re, x_im


def real_inverse(spec_re, spec_im):
    field_count, width, first, second = spec_re.shape
    length = first * second
    cos_a, sin_a = unit_table(first)
    cos_b, sin_b = unit_table(second)
    cos_t, sin_t = twiddle_table(first, second)
    a_re = table_apply(cos_b, spec_re, "mj,fckj->fckm") - table_apply(sin_b, spec_im, "mj,fckj->fckm")
    a_im = table_apply(cos_b, spec_im, "mj,fckj->fckm") + table_apply(sin_b, spec_re, "mj,fckj->fckm")
    b_re = a_re * cos_t - a_im * sin_t
    b_im = a_re * sin_t + a_im * cos_t
    out = table_apply(cos_a, b_re, "nk,fckm->fcnm") - table_apply(sin_a, b_im, "nk,fckm->fcnm")
    return out.reshape(field_count, width, length) * (1.0 / length)


def lag_reverse(signal, axis):
    return jnp.roll(jnp.flip(signal, axis=axis), 1, axis=axis)


def complex_product(left_re, left_im, right_re, right_im):
    return (left_re * right_re - left_im * right_im, left_re * right_im + left_im * right_re)


def to_channels(fields):
    return lax.all_to_all(
        jnp.swapaxes(fields, 1, 2), "seq", split_axis=1, concat_axis=2, tiled=True
    )


def to_rows(fields):
    gathered = lax.all_to_all(fields, "seq", split_axis=2, concat_axis=1, tiled=True)
    return jnp.swapaxes(gathered, 1, 2)


def rep_sum(value):
    count = lax.axis_size("rep")
    total = value
    for shift in range(1, count):
        pairs = [(i, (i + shift) % count) for i in range(count)]
        total = total + lax.ppermute(value, "rep", pairs)
    return total


def chan_reduce_scatter(terms):
    count = lax.axis_size("chan")
    rows, total_width = terms.shape
    pieces = terms.reshape(rows, count, total_width // count).transpose(1, 0, 2)
    received = lax.all_to_all(pieces, "chan", split_axis=0, concat_axis=0, tiled=True)
    total = received[0]
    for index in range(1, count):
        total = total + received[index]
    return total


def on_device(inputs, w_in, w_out, filt_fwd, filt_bwd, skip_gain, cotangent):
    input_rows = inputs[0]
    row_count, chan_width = input_rows.shape
    block_count = chan_width // BLOCK
    input_blocks = input_rows.reshape(row_count, block_count, BLOCK)
    w_blocks = w_in.reshape(block_count, BLOCK, 3, BLOCK)
    grad_rows = cotangent[0]
    piece = lax.all_gather(grad_rows, "chan", axis=1, tiled=True)
    projected = jnp.einsum(
        "mni,nisj->smnj", input_blocks, w_blocks, preferred_element_type=jnp.float32
    )
    projected = projected.reshape(3, row_count, chan_width)
    keys, values, queries = (projected[0], projected[1], projected[2])
    mixed = keys * values
    spread = to_channels(jnp.stack([mixed, filt_fwd, filt_bwd]))
    mixed_cs = spread[0]
    joint_filter = spread[1] + lag_reverse(spread[2], 1)
    spec_re, spec_im = real_spectrum(jnp.stack([mixed_cs, joint_filter]))
    mix_re, mix_im = (spec_re[0], spec_im[0])
    gain_re, gain_im = (spec_re[1], spec_im[1])
    joint_re, joint_im = complex_product(gain_re, gain_im, mix_re, mix_im)
    long_conv = to_rows(real_inverse(joint_re[None], joint_im[None]))[0]
    conv_out = long_conv + skip_gain * mixed
    gated = (queries * conv_out).astype(jnp.bfloat16)
    out_terms = jnp.dot(gated, w_out, preferred_element_type=jnp.float32)
    layer_out = chan_reduce_scatter(out_terms).astype(jnp.bfloat16)
    grad_gated = lax.dot_general(
        piece, w_out, (((1,), (1,)), ((), ())), preferred_element_type=jnp.float32
    )
    grad_wout = lax.dot_general(
        gated, piece, (((0,), (0,)), ((), ())), preferred_element_type=jnp.float32
    )
    grad_queries = grad_gated * conv_out
    grad_conv = grad_gated * queries
    grad_skip = jnp.sum(grad_conv * mixed, axis=0)
    out_width = grad_wout.shape[1]
    skip_row = jnp.pad(grad_skip, (0, out_width - chan_width))[None]
    early_sums = lax.psum(jnp.concatenate([grad_wout, skip_row], axis=0), ("seq", "rep"))
    grad_cs = to_channels(grad_conv[None])
    grad_re, grad_im = real_spectrum(grad_cs)
    grad_re, grad_im = (grad_re[0], grad_im[0])
    back_re, back_im = complex_product(gain_re, -gain_im, grad_re, grad_im)
    cross_re, cross_im = complex_product(grad_re, grad_im, mix_re, -mix_im)
    results = real_inverse(jnp.stack([back_re, cross_re]), jnp.stack([back_im, cross_im]))
    back = to_rows(results[0][None])[0]
    grad_hfwd = rep_sum(results[1])
    grad_hbwd = lag_reverse(grad_hfwd, 1)
    filt_grads = to_rows(jnp.stack([grad_hfwd, grad_hbwd]))
    grad_mixed = back + skip_gain * grad_conv
    grad_pre = jnp.stack([grad_mixed * values, grad_mixed * keys, grad_queries]).astype(
        jnp.bfloat16
    )
    pre_blocks = grad_pre.reshape(3, row_count, block_count, BLOCK)
    d_input = jnp.einsum("smnj,nisj->mni", pre_blocks, w_blocks, preferred_element_type=jnp.float32)
    d_input = d_input.reshape(row_count, chan_width).astype(jnp.bfloat16)
    pre_late, early_sums = lax.optimization_barrier((pre_blocks, early_sums))
    grad_win = jnp.einsum(
        "mni,smnj->nisj", input_blocks, pre_late, preferred_element_type=jnp.float32
    )
    grad_win = grad_win.reshape(chan_width, 3 * BLOCK)
    grad_win = lax.psum(grad_win, ("seq", "rep"))
    grad_wout = early_sums[:chan_width]
    grad_skip = early_sums[chan_width, :chan_width]
    scale = 1.0 / math.sqrt(lax.axis_size("rep") * lax.axis_size("seq") * row_count)
    return (
        layer_out[None],
        d_input[None],
        grad_win * scale,
        grad_wout * scale,
        filt_grads[0] * scale,
        filt_grads[1] * scale,
        grad_skip * scale,
    )


def solution(mesh):
    return jax.shard_map(
        on_device,
        mesh=mesh,
        in_specs=(
            P("rep", "seq", "chan"),
            P("chan", None),
            P("chan", None),
            P("seq", "chan"),
            P("seq", "chan"),
            P("chan"),
            P("rep", "seq", "chan"),
        ),
        out_specs=(
            P("rep", "seq", "chan"),
            P("rep", "seq", "chan"),
            P("chan", None),
            P("chan", None),
            P("seq", "chan"),
            P("seq", "chan"),
            P("chan"),
        ),
        check_vma=False,
    )
```

```python
import math

import jax
import jax.numpy as jnp
import numpy as np
from jax import lax
from jax.sharding import PartitionSpec as P

BLOCK = 512

HIGHEST_PRECISION = lax.Precision.HIGHEST


def factor_split(length):
    second = 256
    return length // second, second


def unit_table(size):
    index_row = np.arange(size)
    angle = 2.0 * np.pi * ((index_row[:, None] * index_row[None, :]) % size) / size
    return (jnp.asarray(np.cos(angle), jnp.float32), jnp.asarray(np.sin(angle), jnp.float32))


def twiddle_table(rows, cols):
    length = rows * cols
    phase = (np.arange(rows)[:, None] * np.arange(cols)[None, :]) % length
    angle = 2.0 * np.pi * phase / length
    return (jnp.asarray(np.cos(angle), jnp.float32), jnp.asarray(np.sin(angle), jnp.float32))


def real_spectrum(signal):
    first, field_count, width, second = signal.shape
    cos_a, sin_a = unit_table(first)
    cos_b, sin_b = unit_table(second)
    cos_t, sin_t = twiddle_table(first, second)
    flat = signal.reshape(first, -1)
    y_re = jnp.dot(cos_a, flat, precision=HIGHEST_PRECISION).reshape(signal.shape)
    y_im = -jnp.dot(sin_a, flat, precision=HIGHEST_PRECISION).reshape(signal.shape)
    cos_t = cos_t[:, None, None, :]
    sin_t = sin_t[:, None, None, :]
    z_re = (y_re * cos_t + y_im * sin_t).reshape(-1, second)
    z_im = (y_im * cos_t - y_re * sin_t).reshape(-1, second)
    x_re = jnp.dot(z_re, cos_b, precision=HIGHEST_PRECISION) + jnp.dot(
        z_im, sin_b, precision=HIGHEST_PRECISION
    )
    x_im = jnp.dot(z_im, cos_b, precision=HIGHEST_PRECISION) - jnp.dot(
        z_re, sin_b, precision=HIGHEST_PRECISION
    )
    return x_re.reshape(signal.shape), x_im.reshape(signal.shape)


def real_inverse(spec_re, spec_im):
    first, field_count, width, second = spec_re.shape
    length = first * second
    cos_a, sin_a = unit_table(first)
    cos_b, sin_b = unit_table(second)
    cos_t, sin_t = twiddle_table(first, second)
    flat_re = spec_re.reshape(-1, second)
    flat_im = spec_im.reshape(-1, second)
    a_re = jnp.dot(flat_re, cos_b, precision=HIGHEST_PRECISION) - jnp.dot(
        flat_im, sin_b, precision=HIGHEST_PRECISION
    )
    a_im = jnp.dot(flat_im, cos_b, precision=HIGHEST_PRECISION) + jnp.dot(
        flat_re, sin_b, precision=HIGHEST_PRECISION
    )
    a_re = a_re.reshape(spec_re.shape)
    a_im = a_im.reshape(spec_re.shape)
    cos_t = cos_t[:, None, None, :]
    sin_t = sin_t[:, None, None, :]
    b_re = (a_re * cos_t - a_im * sin_t).reshape(first, -1)
    b_im = (a_re * sin_t + a_im * cos_t).reshape(first, -1)
    out = jnp.dot(cos_a, b_re, precision=HIGHEST_PRECISION) - jnp.dot(
        sin_a, b_im, precision=HIGHEST_PRECISION
    )
    return out.reshape(spec_re.shape) * (1.0 / length)


def complex_product(left_re, left_im, right_re, right_im):
    return (left_re * right_re - left_im * right_im, left_re * right_im + left_im * right_re)


def to_channels(fields):
    count = lax.axis_size("seq")
    field_count, rows, width = fields.shape
    parts = fields.reshape(field_count, rows, count, width // count).transpose(2, 0, 3, 1)
    return lax.all_to_all(parts, "seq", split_axis=0, concat_axis=0, tiled=True)


def to_rows(fields):
    count, field_count, width, rows = fields.shape
    gathered = lax.all_to_all(fields, "seq", split_axis=0, concat_axis=0, tiled=True)
    return gathered.transpose(1, 3, 0, 2).reshape(field_count, rows, count * width)


def rep_sum(value):
    count = lax.axis_size("rep")
    total = value
    for shift in range(1, count):
        pairs = [(i, (i + shift) % count) for i in range(count)]
        total = total + lax.ppermute(value, "rep", pairs)
    return total


def chan_reduce_scatter(terms):
    count = lax.axis_size("chan")
    rows, total_width = terms.shape
    pieces = terms.reshape(rows, count, total_width // count).transpose(1, 0, 2)
    received = lax.all_to_all(pieces, "chan", split_axis=0, concat_axis=0, tiled=True)
    total = received[0]
    for index in range(1, count):
        total = total + received[index]
    return total


def on_device(inputs, w_in, w_out, filt_fwd, filt_bwd, skip_gain, cotangent):
    input_rows = inputs[0]
    row_count, chan_width = input_rows.shape
    block_count = chan_width // BLOCK
    input_blocks = input_rows.reshape(row_count, block_count, BLOCK)
    w_blocks = w_in.reshape(block_count, BLOCK, 3, BLOCK)
    grad_rows = cotangent[0]
    piece = lax.all_gather(grad_rows, "chan", axis=1, tiled=True)
    projected = jnp.einsum(
        "mni,nisj->smnj", input_blocks, w_blocks, preferred_element_type=jnp.float32
    )
    projected = projected.reshape(3, row_count, chan_width)
    keys, values, queries = (projected[0], projected[1], projected[2])
    mixed = keys * values
    spread = to_channels(jnp.stack([mixed, filt_fwd, filt_bwd]))
    spec_re, spec_im = real_spectrum(spread)
    mix_re, mix_im = (spec_re[:, 0], spec_im[:, 0])
    gain_re = spec_re[:, 1] + spec_re[:, 2]
    gain_im = spec_im[:, 1] - spec_im[:, 2]
    joint_re, joint_im = complex_product(gain_re, gain_im, mix_re, mix_im)
    long_conv = to_rows(real_inverse(joint_re[:, None], joint_im[:, None]))[0]
    conv_out = long_conv + skip_gain * mixed
    gated = (queries * conv_out).astype(jnp.bfloat16)
    out_terms = jnp.dot(gated, w_out, preferred_element_type=jnp.float32)
    layer_out = chan_reduce_scatter(out_terms).astype(jnp.bfloat16)
    grad_gated = lax.dot_general(
        piece, w_out, (((1,), (1,)), ((), ())), preferred_element_type=jnp.float32
    )
    grad_wout = lax.dot_general(
        gated, piece, (((0,), (0,)), ((), ())), preferred_element_type=jnp.float32
    )
    grad_queries = grad_gated * conv_out
    grad_conv = grad_gated * queries
    grad_skip = jnp.sum(grad_conv * mixed, axis=0)
    grad_re, grad_im = real_spectrum(to_channels(grad_conv[None]))
    grad_re, grad_im = (grad_re[:, 0], grad_im[:, 0])
    back_re, back_im = complex_product(gain_re, -gain_im, grad_re, grad_im)
    cross_re, cross_im = complex_product(grad_re, grad_im, mix_re, -mix_im)
    results = real_inverse(
        jnp.stack([back_re, cross_re, cross_re], axis=1),
        jnp.stack([back_im, cross_im, -cross_im], axis=1),
    )
    back = to_rows(results[:, :1])[0]
    filt_grads = to_rows(rep_sum(results[:, 1:]))
    grad_mixed = back + skip_gain * grad_conv
    grad_pre = jnp.stack([grad_mixed * values, grad_mixed * keys, grad_queries]).astype(
        jnp.bfloat16
    )
    pre_blocks = grad_pre.reshape(3, row_count, block_count, BLOCK)
    d_input = jnp.einsum("smnj,nisj->mni", pre_blocks, w_blocks, preferred_element_type=jnp.float32)
    d_input = d_input.reshape(row_count, chan_width).astype(jnp.bfloat16)
    grad_win = jnp.einsum(
        "mni,smnj->nisj", input_blocks, pre_blocks, preferred_element_type=jnp.float32
    )
    grad_win = grad_win.reshape(chan_width, 3 * BLOCK)
    out_width = grad_wout.shape[1]
    skip_row = jnp.pad(grad_skip, (0, out_width - chan_width))[None]
    sums = lax.psum((grad_win, jnp.concatenate([grad_wout, skip_row], axis=0)), ("seq", "rep"))
    grad_win = sums[0]
    grad_wout = sums[1][:chan_width]
    grad_skip = sums[1][chan_width, :chan_width]
    scale = 1.0 / math.sqrt(lax.axis_size("rep") * lax.axis_size("seq") * row_count)
    return (
        layer_out[None],
        d_input[None],
        grad_win * scale,
        grad_wout * scale,
        filt_grads[0] * scale,
        filt_grads[1] * scale,
        grad_skip * scale,
    )


def solution(mesh):
    return jax.shard_map(
        on_device,
        mesh=mesh,
        in_specs=(
            P("rep", "seq", "chan"),
            P("chan", None),
            P("chan", None),
            P("seq", "chan"),
            P("seq", "chan"),
            P("chan"),
            P("rep", "seq", "chan"),
        ),
        out_specs=(
            P("rep", "seq", "chan"),
            P("rep", "seq", "chan"),
            P("chan", None),
            P("chan", None),
            P("seq", "chan"),
            P("seq", "chan"),
            P("chan"),
        ),
        check_vma=False,
    )
```

```python
import math

import jax
import jax.numpy as jnp
import numpy as np
from jax import lax
from jax.sharding import PartitionSpec as P

BLOCK = 512

HIGHEST_PRECISION = lax.Precision.HIGHEST


def factor_split(length):
    second = 256
    return length // second, second


def unit_table(size):
    index_row = np.arange(size)
    angle = 2.0 * np.pi * ((index_row[:, None] * index_row[None, :]) % size) / size
    return (jnp.asarray(np.cos(angle), jnp.float32), jnp.asarray(np.sin(angle), jnp.float32))


def twiddle_table(rows, cols):
    length = rows * cols
    phase = (np.arange(rows)[:, None] * np.arange(cols)[None, :]) % length
    angle = 2.0 * np.pi * phase / length
    return (jnp.asarray(np.cos(angle), jnp.float32), jnp.asarray(np.sin(angle), jnp.float32))


def real_spectrum(signal):
    first, field_count, width, second = signal.shape
    cos_a, sin_a = unit_table(first)
    cos_b, sin_b = unit_table(second)
    cos_t, sin_t = twiddle_table(first, second)
    flat = signal.reshape(first, -1)
    y_re = jnp.dot(cos_a, flat, precision=HIGHEST_PRECISION).reshape(signal.shape)
    y_im = -jnp.dot(sin_a, flat, precision=HIGHEST_PRECISION).reshape(signal.shape)
    cos_t = cos_t[:, None, None, :]
    sin_t = sin_t[:, None, None, :]
    z_re = (y_re * cos_t + y_im * sin_t).reshape(-1, second)
    z_im = (y_im * cos_t - y_re * sin_t).reshape(-1, second)
    x_re = jnp.dot(z_re, cos_b, precision=HIGHEST_PRECISION) + jnp.dot(
        z_im, sin_b, precision=HIGHEST_PRECISION
    )
    x_im = jnp.dot(z_im, cos_b, precision=HIGHEST_PRECISION) - jnp.dot(
        z_re, sin_b, precision=HIGHEST_PRECISION
    )
    return x_re.reshape(signal.shape), x_im.reshape(signal.shape)


def real_inverse(spec_re, spec_im):
    first, field_count, width, second = spec_re.shape
    length = first * second
    cos_a, sin_a = unit_table(first)
    cos_b, sin_b = unit_table(second)
    cos_t, sin_t = twiddle_table(first, second)
    flat_re = spec_re.reshape(-1, second)
    flat_im = spec_im.reshape(-1, second)
    a_re = jnp.dot(flat_re, cos_b, precision=HIGHEST_PRECISION) - jnp.dot(
        flat_im, sin_b, precision=HIGHEST_PRECISION
    )
    a_im = jnp.dot(flat_im, cos_b, precision=HIGHEST_PRECISION) + jnp.dot(
        flat_re, sin_b, precision=HIGHEST_PRECISION
    )
    a_re = a_re.reshape(spec_re.shape)
    a_im = a_im.reshape(spec_re.shape)
    cos_t = cos_t[:, None, None, :]
    sin_t = sin_t[:, None, None, :]
    b_re = (a_re * cos_t - a_im * sin_t).reshape(first, -1)
    b_im = (a_re * sin_t + a_im * cos_t).reshape(first, -1)
    out = jnp.dot(cos_a, b_re, precision=HIGHEST_PRECISION) - jnp.dot(
        sin_a, b_im, precision=HIGHEST_PRECISION
    )
    return out.reshape(spec_re.shape) * (1.0 / length)


def complex_product(left_re, left_im, right_re, right_im):
    return (left_re * right_re - left_im * right_im, left_re * right_im + left_im * right_re)


def to_channels(fields):
    count = lax.axis_size("seq")
    field_count, rows, width = fields.shape
    parts = fields.reshape(field_count, rows, count, width // count).transpose(2, 0, 3, 1)
    return lax.all_to_all(parts, "seq", split_axis=0, concat_axis=0, tiled=True)


def to_rows(fields):
    count, field_count, width, rows = fields.shape
    gathered = lax.all_to_all(fields, "seq", split_axis=0, concat_axis=0, tiled=True)
    return gathered.transpose(1, 3, 0, 2).reshape(field_count, rows, count * width)


def rep_sum(value):
    count = lax.axis_size("rep")
    total = value
    for shift in range(1, count):
        pairs = [(i, (i + shift) % count) for i in range(count)]
        total = total + lax.ppermute(value, "rep", pairs)
    return total


def chan_reduce_scatter(terms):
    count = lax.axis_size("chan")
    rows, total_width = terms.shape
    pieces = terms.reshape(rows, count, total_width // count).transpose(1, 0, 2)
    received = lax.all_to_all(pieces, "chan", split_axis=0, concat_axis=0, tiled=True)
    total = received[0]
    for index in range(1, count):
        total = total + received[index]
    return total


def on_device(inputs, w_in, w_out, filt_fwd, filt_bwd, skip_gain, cotangent):
    input_rows = inputs[0]
    row_count, chan_width = input_rows.shape
    block_count = chan_width // BLOCK
    input_blocks = input_rows.reshape(row_count, block_count, BLOCK)
    w_blocks = w_in.reshape(block_count, BLOCK, 3, BLOCK)
    grad_rows = cotangent[0]
    piece = lax.all_gather(grad_rows, "chan", axis=1, tiled=True)
    projected = jnp.einsum(
        "mni,nisj->smnj", input_blocks, w_blocks, preferred_element_type=jnp.float32
    )
    projected = projected.reshape(3, row_count, chan_width)
    keys, values, queries = (projected[0], projected[1], projected[2])
    mixed = keys * values
    spread = to_channels(jnp.stack([mixed, filt_fwd, filt_bwd]))
    spec_re, spec_im = real_spectrum(spread)
    mix_re, mix_im = (spec_re[:, 0], spec_im[:, 0])
    gain_re = spec_re[:, 1] + spec_re[:, 2]
    gain_im = spec_im[:, 1] - spec_im[:, 2]
    grad_gated = lax.dot_general(
        piece, w_out, (((1,), (1,)), ((), ())), preferred_element_type=jnp.float32
    )
    grad_conv = grad_gated * queries
    grad_re, grad_im = real_spectrum(to_channels(grad_conv[None]))
    grad_re, grad_im = (grad_re[:, 0], grad_im[:, 0])
    joint_re, joint_im = complex_product(gain_re, gain_im, mix_re, mix_im)
    back_re, back_im = complex_product(gain_re, -gain_im, grad_re, grad_im)
    both = to_rows(
        real_inverse(
            jnp.stack([joint_re, back_re], axis=1), jnp.stack([joint_im, back_im], axis=1)
        )
    )
    long_conv = both[0]
    back = both[1]
    cross_re, cross_im = complex_product(grad_re, grad_im, mix_re, -mix_im)
    cross = real_inverse(
        jnp.stack([cross_re, cross_re], axis=1), jnp.stack([cross_im, -cross_im], axis=1)
    )
    scale = 1.0 / math.sqrt(lax.axis_size("rep") * lax.axis_size("seq") * row_count)
    filt_grads = to_rows(rep_sum(cross * scale))
    conv_out = long_conv + skip_gain * mixed
    gated = (queries * conv_out).astype(jnp.bfloat16)
    out_terms = jnp.dot(gated, w_out, preferred_element_type=jnp.float32)
    layer_out = chan_reduce_scatter(out_terms).astype(jnp.bfloat16)
    grad_wout = lax.dot_general(
        gated, piece, (((0,), (0,)), ((), ())), preferred_element_type=jnp.float32
    )
    grad_queries = grad_gated * conv_out
    grad_skip = jnp.sum(grad_conv * mixed, axis=0)
    grad_mixed = back + skip_gain * grad_conv
    grad_pre = jnp.stack([grad_mixed * values, grad_mixed * keys, grad_queries]).astype(
        jnp.bfloat16
    )
    pre_blocks = grad_pre.reshape(3, row_count, block_count, BLOCK)
    d_input = jnp.einsum("smnj,nisj->mni", pre_blocks, w_blocks, preferred_element_type=jnp.float32)
    d_input = d_input.reshape(row_count, chan_width).astype(jnp.bfloat16)
    grad_win = jnp.einsum(
        "mni,smnj->nisj", input_blocks, pre_blocks, preferred_element_type=jnp.float32
    )
    grad_win = grad_win.reshape(chan_width, 3 * BLOCK) * scale
    out_width = grad_wout.shape[1]
    skip_row = jnp.pad(grad_skip, (0, out_width - chan_width))[None]
    joined = jnp.concatenate([grad_wout, skip_row], axis=0) * scale
    grad_win, joined = lax.psum((grad_win, joined), ("seq", "rep"))
    return (
        layer_out[None],
        d_input[None],
        grad_win,
        joined[:chan_width],
        filt_grads[0],
        filt_grads[1],
        joined[chan_width, :chan_width],
    )


def solution(mesh):
    return jax.shard_map(
        on_device,
        mesh=mesh,
        in_specs=(
            P("rep", "seq", "chan"),
            P("chan", None),
            P("chan", None),
            P("seq", "chan"),
            P("seq", "chan"),
            P("chan"),
            P("rep", "seq", "chan"),
        ),
        out_specs=(
            P("rep", "seq", "chan"),
            P("rep", "seq", "chan"),
            P("chan", None),
            P("chan", None),
            P("seq", "chan"),
            P("seq", "chan"),
            P("chan"),
        ),
        check_vma=False,
    )
```

```python
import math

import jax
import jax.numpy as jnp
import numpy as np
from jax import lax
from jax.sharding import PartitionSpec as P

BLOCK = 512

TABLE_PRECISION = lax.Precision.HIGH


def factor_split(length):
    second = 256
    return length // second, second


def unit_table(size):
    index_row = np.arange(size)
    angle = 2.0 * np.pi * ((index_row[:, None] * index_row[None, :]) % size) / size
    return (jnp.asarray(np.cos(angle), jnp.float32), jnp.asarray(np.sin(angle), jnp.float32))


def twiddle_table(rows, cols):
    length = rows * cols
    phase = (np.arange(rows)[:, None] * np.arange(cols)[None, :]) % length
    angle = 2.0 * np.pi * phase / length
    return (jnp.asarray(np.cos(angle), jnp.float32), jnp.asarray(np.sin(angle), jnp.float32))


def lead_apply(table, fields):
    return jnp.einsum("kn,nrm->krm", table, fields, precision=TABLE_PRECISION)


def minor_apply(fields, table):
    return jnp.einsum("krm,mj->krj", fields, table, precision=TABLE_PRECISION)


def real_spectrum(signal):
    first, field_count, width, second = signal.shape
    cos_a, sin_a = unit_table(first)
    cos_b, sin_b = unit_table(second)
    cos_t, sin_t = twiddle_table(first, second)
    grid = signal.reshape(first, field_count * width, second)
    y_re = lead_apply(cos_a, grid)
    y_im = lead_apply(-sin_a, grid)
    cos_t = cos_t[:, None, :]
    sin_t = sin_t[:, None, :]
    z_re = y_re * cos_t + y_im * sin_t
    z_im = y_im * cos_t - y_re * sin_t
    x_re = minor_apply(z_re, cos_b) + minor_apply(z_im, sin_b)
    x_im = minor_apply(z_im, cos_b) + minor_apply(z_re, -sin_b)
    return x_re.reshape(signal.shape), x_im.reshape(signal.shape)


def real_inverse(spec_re, spec_im):
    first, field_count, width, second = spec_re.shape
    length = first * second
    cos_a, sin_a = unit_table(first)
    cos_b, sin_b = unit_table(second)
    cos_t, sin_t = twiddle_table(first, second)
    flat_re = spec_re.reshape(first, field_count * width, second)
    flat_im = spec_im.reshape(first, field_count * width, second)
    a_re = minor_apply(flat_re, cos_b) + minor_apply(flat_im, -sin_b)
    a_im = minor_apply(flat_im, cos_b) + minor_apply(flat_re, sin_b)
    cos_t = cos_t[:, None, :] * (1.0 / length)
    sin_t = sin_t[:, None, :] * (1.0 / length)
    b_re = a_re * cos_t - a_im * sin_t
    b_im = a_re * sin_t + a_im * cos_t
    out = lead_apply(cos_a, b_re) + lead_apply(-sin_a, b_im)
    return out.reshape(spec_re.shape)


def complex_product(left_re, left_im, right_re, right_im):
    return (left_re * right_re - left_im * right_im, left_re * right_im + left_im * right_re)


def to_channels(fields):
    count = lax.axis_size("seq")
    field_count, rows, width = fields.shape
    parts = fields.reshape(field_count, rows, count, width // count).transpose(2, 0, 3, 1)
    return lax.all_to_all(parts, "seq", split_axis=0, concat_axis=0, tiled=True)


def to_rows(fields):
    count, field_count, width, rows = fields.shape
    gathered = lax.all_to_all(fields, "seq", split_axis=0, concat_axis=0, tiled=True)
    return gathered.transpose(1, 3, 0, 2).reshape(field_count, rows, count * width)


def rep_sum(value):
    count = lax.axis_size("rep")
    total = value
    for shift in range(1, count):
        pairs = [(i, (i + shift) % count) for i in range(count)]
        total = total + lax.ppermute(value, "rep", pairs)
    return total


def chan_reduce_scatter(terms):
    count = lax.axis_size("chan")
    rows, total_width = terms.shape
    pieces = terms.reshape(rows, count, total_width // count).transpose(1, 0, 2)
    received = lax.all_to_all(pieces, "chan", split_axis=0, concat_axis=0, tiled=True)
    total = received[0]
    for index in range(1, count):
        total = total + received[index]
    return total


def on_device(inputs, w_in, w_out, filt_fwd, filt_bwd, skip_gain, cotangent):
    input_rows = inputs[0]
    row_count, chan_width = input_rows.shape
    block_count = chan_width // BLOCK
    input_blocks = input_rows.reshape(row_count, block_count, BLOCK)
    w_blocks = w_in.reshape(block_count, BLOCK, 3, BLOCK)
    grad_rows = cotangent[0]
    piece = lax.all_gather(grad_rows, "chan", axis=1, tiled=True)
    projected = jnp.einsum(
        "mni,nisj->smnj", input_blocks, w_blocks, preferred_element_type=jnp.float32
    )
    projected = projected.reshape(3, row_count, chan_width)
    keys, values, queries = (projected[0], projected[1], projected[2])
    mixed = keys * values
    spread = to_channels(jnp.stack([mixed, filt_fwd, filt_bwd]))
    spec_re, spec_im = real_spectrum(spread)
    mix_re, mix_im = (spec_re[:, 0], spec_im[:, 0])
    gain_re = spec_re[:, 1] + spec_re[:, 2]
    gain_im = spec_im[:, 1] - spec_im[:, 2]
    grad_gated = lax.dot_general(
        piece, w_out, (((1,), (1,)), ((), ())), preferred_element_type=jnp.float32
    )
    grad_conv = grad_gated * queries
    grad_cs = to_channels(grad_conv[None])
    grad_re, grad_im = real_spectrum(grad_cs)
    grad_re, grad_im = (grad_re[:, 0], grad_im[:, 0])
    joint_re, joint_im = complex_product(gain_re, gain_im, mix_re, mix_im)
    back_re, back_im = complex_product(gain_re, -gain_im, grad_re, grad_im)
    both = to_rows(
        real_inverse(
            jnp.stack([joint_re, back_re], axis=1), jnp.stack([joint_im, back_im], axis=1)
        )
    )
    long_conv = both[0]
    back = both[1]
    cross_re, cross_im = complex_product(grad_re, grad_im, mix_re, -mix_im)
    cross = real_inverse(
        jnp.stack([cross_re, cross_re], axis=1), jnp.stack([cross_im, -cross_im], axis=1)
    )
    scale = 1.0 / math.sqrt(lax.axis_size("rep") * lax.axis_size("seq") * row_count)
    skip_part = jnp.sum(grad_cs * spread[:, :1], axis=(0, 3))
    skip_field = jnp.broadcast_to(skip_part[None, :, :, None], grad_cs.shape)
    filt_grads = to_rows(rep_sum(jnp.concatenate([cross, skip_field], axis=1) * scale))
    conv_out = long_conv + skip_gain * mixed
    gated = (queries * conv_out).astype(jnp.bfloat16)
    out_terms = jnp.dot(gated, w_out, preferred_element_type=jnp.float32)
    layer_out = chan_reduce_scatter(out_terms).astype(jnp.bfloat16)
    grad_wout = lax.dot_general(
        gated, piece, (((0,), (0,)), ((), ())), preferred_element_type=jnp.float32
    )
    grad_queries = grad_gated * conv_out
    grad_mixed = back + skip_gain * grad_conv
    grad_pre = jnp.stack([grad_mixed * values, grad_mixed * keys, grad_queries]).astype(
        jnp.bfloat16
    )
    pre_blocks = grad_pre.reshape(3, row_count, block_count, BLOCK)
    d_input = jnp.einsum("smnj,nisj->mni", pre_blocks, w_blocks, preferred_element_type=jnp.float32)
    d_input = d_input.reshape(row_count, chan_width).astype(jnp.bfloat16)
    grad_win = jnp.einsum(
        "mni,smnj->nisj", input_blocks, pre_blocks, preferred_element_type=jnp.float32
    )
    grad_win = grad_win.reshape(chan_width, 3 * BLOCK) * scale
    grad_win, grad_wout = lax.psum((grad_win, grad_wout * scale), ("seq", "rep"))
    return (
        layer_out[None],
        d_input[None],
        grad_win,
        grad_wout,
        filt_grads[0],
        filt_grads[1],
        filt_grads[2, 0],
    )


def solution(mesh):
    return jax.shard_map(
        on_device,
        mesh=mesh,
        in_specs=(
            P("rep", "seq", "chan"),
            P("chan", None),
            P("chan", None),
            P("seq", "chan"),
            P("seq", "chan"),
            P("chan"),
            P("rep", "seq", "chan"),
        ),
        out_specs=(
            P("rep", "seq", "chan"),
            P("rep", "seq", "chan"),
            P("chan", None),
            P("chan", None),
            P("seq", "chan"),
            P("seq", "chan"),
            P("chan"),
        ),
        check_vma=False,
    )
```

```python
import math

import jax
import jax.numpy as jnp
import numpy as np
from jax import lax
from jax.sharding import PartitionSpec as P

BLOCK = 512

TABLE_PRECISION = lax.Precision.HIGH


def factor_split(length):
    second = 256
    return length // second, second


def unit_table(size):
    index_row = np.arange(size)
    angle = 2.0 * np.pi * ((index_row[:, None] * index_row[None, :]) % size) / size
    return (jnp.asarray(np.cos(angle), jnp.float32), jnp.asarray(np.sin(angle), jnp.float32))


def twiddle_table(rows, cols):
    length = rows * cols
    phase = (np.arange(rows)[:, None] * np.arange(cols)[None, :]) % length
    angle = 2.0 * np.pi * phase / length
    return (jnp.asarray(np.cos(angle), jnp.float32), jnp.asarray(np.sin(angle), jnp.float32))


def lead_apply(table, fields):
    return jnp.einsum("kn,nrm->krm", table, fields, precision=TABLE_PRECISION)


def minor_apply(fields, table):
    return jnp.einsum("krm,mj->krj", fields, table, precision=TABLE_PRECISION)


def real_spectrum(signal):
    first, field_count, width, second = signal.shape
    cos_a, sin_a = unit_table(first)
    cos_b, sin_b = unit_table(second)
    cos_t, sin_t = twiddle_table(first, second)
    grid = signal.reshape(first, field_count * width, second)
    y_re = lead_apply(cos_a, grid)
    y_im = lead_apply(-sin_a, grid)
    cos_t = cos_t[:, None, :]
    sin_t = sin_t[:, None, :]
    z_re = y_re * cos_t + y_im * sin_t
    z_im = y_im * cos_t - y_re * sin_t
    x_re = minor_apply(z_re, cos_b) + minor_apply(z_im, sin_b)
    x_im = minor_apply(z_im, cos_b) + minor_apply(z_re, -sin_b)
    return x_re.reshape(signal.shape), x_im.reshape(signal.shape)


def real_inverse(spec_re, spec_im):
    first, field_count, width, second = spec_re.shape
    length = first * second
    cos_a, sin_a = unit_table(first)
    cos_b, sin_b = unit_table(second)
    cos_t, sin_t = twiddle_table(first, second)
    flat_re = spec_re.reshape(first, field_count * width, second)
    flat_im = spec_im.reshape(first, field_count * width, second)
    a_re = minor_apply(flat_re, cos_b) + minor_apply(flat_im, -sin_b)
    a_im = minor_apply(flat_im, cos_b) + minor_apply(flat_re, sin_b)
    cos_t = cos_t[:, None, :] * (1.0 / length)
    sin_t = sin_t[:, None, :] * (1.0 / length)
    b_re = a_re * cos_t - a_im * sin_t
    b_im = a_re * sin_t + a_im * cos_t
    out = lead_apply(cos_a, b_re) + lead_apply(-sin_a, b_im)
    return out.reshape(spec_re.shape)


def complex_product(left_re, left_im, right_re, right_im):
    return (left_re * right_re - left_im * right_im, left_re * right_im + left_im * right_re)


def to_channels(fields):
    count = lax.axis_size("seq")
    field_count, rows, width = fields.shape
    parts = fields.reshape(field_count, rows, count, width // count).transpose(2, 0, 3, 1)
    return lax.all_to_all(parts, "seq", split_axis=0, concat_axis=0, tiled=True)


def to_rows(fields):
    count, field_count, width, rows = fields.shape
    gathered = lax.all_to_all(fields, "seq", split_axis=0, concat_axis=0, tiled=True)
    return gathered.transpose(1, 3, 0, 2).reshape(field_count, rows, count * width)


def rep_sum(value):
    count = lax.axis_size("rep")
    total = value
    for shift in range(1, count):
        pairs = [(i, (i + shift) % count) for i in range(count)]
        total = total + lax.ppermute(value, "rep", pairs)
    return total


def chan_reduce_scatter(terms):
    count = lax.axis_size("chan")
    rows, total_width = terms.shape
    pieces = terms.reshape(rows, count, total_width // count).transpose(1, 0, 2)
    received = lax.all_to_all(pieces, "chan", split_axis=0, concat_axis=0, tiled=True)
    total = received[0]
    for index in range(1, count):
        total = total + received[index]
    return total


def on_device(inputs, w_in, w_out, filt_fwd, filt_bwd, skip_gain, cotangent):
    input_rows = inputs[0]
    row_count, chan_width = input_rows.shape
    block_count = chan_width // BLOCK
    input_blocks = input_rows.reshape(row_count, block_count, BLOCK)
    w_blocks = w_in.reshape(block_count, BLOCK, 3, BLOCK)
    grad_rows = cotangent[0]
    chan_count = lax.axis_size("chan")
    copies = jnp.broadcast_to(grad_rows[None], (chan_count,) + grad_rows.shape)
    gathered = lax.all_to_all(copies, "chan", split_axis=0, concat_axis=0, tiled=True)
    piece = gathered.transpose(1, 0, 2).reshape(grad_rows.shape[0], -1)
    projected = jnp.einsum(
        "mni,nisj->smnj", input_blocks, w_blocks, preferred_element_type=jnp.float32
    )
    projected = projected.reshape(3, row_count, chan_width)
    keys, values, queries = (projected[0], projected[1], projected[2])
    mixed = keys * values
    grad_gated = lax.dot_general(
        piece, w_out, (((1,), (1,)), ((), ())), preferred_element_type=jnp.float32
    )
    grad_conv = grad_gated * queries
    spread = to_channels(jnp.stack([mixed, filt_fwd, filt_bwd, grad_conv]))
    spec_re, spec_im = real_spectrum(spread)
    mix_re, mix_im = (spec_re[:, 0], spec_im[:, 0])
    gain_re = spec_re[:, 1] + spec_re[:, 2]
    gain_im = spec_im[:, 1] - spec_im[:, 2]
    grad_re, grad_im = (spec_re[:, 3], spec_im[:, 3])
    grad_cs = spread[:, 3:]
    joint_re, joint_im = complex_product(gain_re, gain_im, mix_re, mix_im)
    back_re, back_im = complex_product(gain_re, -gain_im, grad_re, grad_im)
    both = to_rows(
        real_inverse(
            jnp.stack([joint_re, back_re], axis=1), jnp.stack([joint_im, back_im], axis=1)
        )
    )
    long_conv = both[0]
    back = both[1]
    cross_re, cross_im = complex_product(grad_re, grad_im, mix_re, -mix_im)
    cross = real_inverse(
        jnp.stack([cross_re, cross_re], axis=1), jnp.stack([cross_im, -cross_im], axis=1)
    )
    scale = 1.0 / math.sqrt(lax.axis_size("rep") * lax.axis_size("seq") * row_count)
    skip_part = jnp.sum(grad_cs * spread[:, :1], axis=(0, 3))
    skip_field = jnp.broadcast_to(skip_part[None, :, :, None], grad_cs.shape)
    filt_grads = to_rows(rep_sum(jnp.concatenate([cross, skip_field], axis=1) * scale))
    conv_out = long_conv + skip_gain * mixed
    gated = (queries * conv_out).astype(jnp.bfloat16)
    out_terms = jnp.dot(gated, w_out, preferred_element_type=jnp.float32)
    layer_out = chan_reduce_scatter(out_terms).astype(jnp.bfloat16)
    grad_wout = lax.dot_general(
        gated, piece, (((0,), (0,)), ((), ())), preferred_element_type=jnp.float32
    )
    grad_queries = grad_gated * conv_out
    grad_mixed = back + skip_gain * grad_conv
    grad_pre = jnp.stack([grad_mixed * values, grad_mixed * keys, grad_queries]).astype(
        jnp.bfloat16
    )
    pre_blocks = grad_pre.reshape(3, row_count, block_count, BLOCK)
    d_input = jnp.einsum("smnj,nisj->mni", pre_blocks, w_blocks, preferred_element_type=jnp.float32)
    d_input = d_input.reshape(row_count, chan_width).astype(jnp.bfloat16)
    grad_win = jnp.einsum(
        "mni,smnj->nisj", input_blocks, pre_blocks, preferred_element_type=jnp.float32
    )
    grad_win = grad_win.reshape(chan_width, 3 * BLOCK) * scale
    grad_win, grad_wout = lax.psum((grad_win, grad_wout * scale), ("seq", "rep"))
    return (
        layer_out[None],
        d_input[None],
        grad_win,
        grad_wout,
        filt_grads[0],
        filt_grads[1],
        filt_grads[2, 0],
    )


def solution(mesh):
    return jax.shard_map(
        on_device,
        mesh=mesh,
        in_specs=(
            P("rep", "seq", "chan"),
            P("chan", None),
            P("chan", None),
            P("seq", "chan"),
            P("seq", "chan"),
            P("chan"),
            P("rep", "seq", "chan"),
        ),
        out_specs=(
            P("rep", "seq", "chan"),
            P("rep", "seq", "chan"),
            P("chan", None),
            P("chan", None),
            P("seq", "chan"),
            P("seq", "chan"),
            P("chan"),
        ),
        check_vma=False,
    )
```

```python
import math

import jax
import jax.numpy as jnp
import numpy as np
from jax import lax
from jax.sharding import PartitionSpec as P

BLOCK = 512

TABLE_PRECISION = lax.Precision.HIGH


def factor_split(length):
    second = 256
    return length // second, second


def unit_table(size):
    index_row = np.arange(size)
    angle = 2.0 * np.pi * ((index_row[:, None] * index_row[None, :]) % size) / size
    return (jnp.asarray(np.cos(angle), jnp.float32), jnp.asarray(np.sin(angle), jnp.float32))


def twiddle_table(rows, cols):
    length = rows * cols
    phase = (np.arange(rows)[:, None] * np.arange(cols)[None, :]) % length
    angle = 2.0 * np.pi * phase / length
    return (jnp.asarray(np.cos(angle), jnp.float32), jnp.asarray(np.sin(angle), jnp.float32))


def lead_apply(table, fields):
    return jnp.einsum("kn,nrm->krm", table, fields, precision=TABLE_PRECISION)


def minor_apply(fields, table):
    return jnp.einsum("krm,mj->krj", fields, table, precision=TABLE_PRECISION)


def real_spectrum(signal):
    first, field_count, width, second = signal.shape
    cos_a, sin_a = unit_table(first)
    cos_b, sin_b = unit_table(second)
    cos_t, sin_t = twiddle_table(first, second)
    grid = signal.reshape(first, field_count * width, second)
    y_re = lead_apply(cos_a, grid)
    y_im = lead_apply(-sin_a, grid)
    cos_t = cos_t[:, None, :]
    sin_t = sin_t[:, None, :]
    z_re = y_re * cos_t + y_im * sin_t
    z_im = y_im * cos_t - y_re * sin_t
    x_re = minor_apply(z_re, cos_b) + minor_apply(z_im, sin_b)
    x_im = minor_apply(z_im, cos_b) + minor_apply(z_re, -sin_b)
    return x_re.reshape(signal.shape), x_im.reshape(signal.shape)


def real_inverse(spec_re, spec_im):
    first, field_count, width, second = spec_re.shape
    length = first * second
    cos_a, sin_a = unit_table(first)
    cos_b, sin_b = unit_table(second)
    cos_t, sin_t = twiddle_table(first, second)
    flat_re = spec_re.reshape(first, field_count * width, second)
    flat_im = spec_im.reshape(first, field_count * width, second)
    a_re = minor_apply(flat_re, cos_b) + minor_apply(flat_im, -sin_b)
    a_im = minor_apply(flat_im, cos_b) + minor_apply(flat_re, sin_b)
    cos_t = cos_t[:, None, :] * (1.0 / length)
    sin_t = sin_t[:, None, :] * (1.0 / length)
    b_re = a_re * cos_t - a_im * sin_t
    b_im = a_re * sin_t + a_im * cos_t
    out = lead_apply(cos_a, b_re) + lead_apply(-sin_a, b_im)
    return out.reshape(spec_re.shape)


def complex_product(left_re, left_im, right_re, right_im):
    return (left_re * right_re - left_im * right_im, left_re * right_im + left_im * right_re)


def to_channels(fields):
    count = lax.axis_size("seq")
    field_count, rows, width = fields.shape
    parts = fields.reshape(field_count, rows, count, width // count).transpose(2, 0, 3, 1)
    return lax.all_to_all(parts, "seq", split_axis=0, concat_axis=0, tiled=True)


def to_rows(fields):
    count, field_count, width, rows = fields.shape
    gathered = lax.all_to_all(fields, "seq", split_axis=0, concat_axis=0, tiled=True)
    return gathered.transpose(1, 3, 0, 2).reshape(field_count, rows, count * width)


def rep_sum(value):
    count = lax.axis_size("rep")
    total = value
    for shift in range(1, count):
        pairs = [(i, (i + shift) % count) for i in range(count)]
        total = total + lax.ppermute(value, "rep", pairs)
    return total


def chan_reduce_scatter(terms):
    count = lax.axis_size("chan")
    rows, total_width = terms.shape
    pieces = terms.reshape(rows, count, total_width // count).transpose(1, 0, 2)
    received = lax.all_to_all(pieces, "chan", split_axis=0, concat_axis=0, tiled=True)
    total = received[0]
    for index in range(1, count):
        total = total + received[index]
    return total


def on_device(inputs, w_in, w_out, filt_fwd, filt_bwd, skip_gain, cotangent):
    input_rows = inputs[0]
    row_count, chan_width = input_rows.shape
    block_count = chan_width // BLOCK
    input_blocks = input_rows.reshape(row_count, block_count, BLOCK)
    w_blocks = w_in.reshape(block_count, BLOCK, 3, BLOCK)
    grad_rows = cotangent[0]
    chan_count = lax.axis_size("chan")
    copies = jnp.broadcast_to(grad_rows[None], (chan_count,) + grad_rows.shape)
    gathered = lax.all_to_all(copies, "chan", split_axis=0, concat_axis=0, tiled=True)
    piece = gathered.transpose(1, 0, 2).reshape(grad_rows.shape[0], -1)
    projected = jnp.einsum(
        "mni,nisj->smnj", input_blocks, w_blocks, preferred_element_type=jnp.float32
    )
    projected = projected.reshape(3, row_count, chan_width)
    keys, values, queries = (projected[0], projected[1], projected[2])
    mixed = keys * values
    grad_gated = lax.dot_general(
        piece, w_out, (((1,), (1,)), ((), ())), preferred_element_type=jnp.float32
    )
    grad_conv = grad_gated * queries
    filt_re, filt_im = real_spectrum(to_channels(jnp.stack([filt_fwd, filt_bwd])))
    gain_re = filt_re[:, 0] + filt_re[:, 1]
    gain_im = filt_im[:, 0] - filt_im[:, 1]
    spread = to_channels(jnp.stack([mixed, grad_conv]))
    spec_re, spec_im = real_spectrum(spread)
    mix_re, mix_im = (spec_re[:, 0], spec_im[:, 0])
    grad_re, grad_im = (spec_re[:, 1], spec_im[:, 1])
    grad_cs = spread[:, 1:]
    joint_re, joint_im = complex_product(gain_re, gain_im, mix_re, mix_im)
    back_re, back_im = complex_product(gain_re, -gain_im, grad_re, grad_im)
    both = to_rows(
        real_inverse(
            jnp.stack([joint_re, back_re], axis=1), jnp.stack([joint_im, back_im], axis=1)
        )
    )
    long_conv = both[0]
    back = both[1]
    cross_re, cross_im = complex_product(grad_re, grad_im, mix_re, -mix_im)
    cross = real_inverse(
        jnp.stack([cross_re, cross_re], axis=1), jnp.stack([cross_im, -cross_im], axis=1)
    )
    scale = 1.0 / math.sqrt(lax.axis_size("rep") * lax.axis_size("seq") * row_count)
    skip_part = jnp.sum(grad_cs * spread[:, :1], axis=(0, 3))
    skip_field = jnp.broadcast_to(skip_part[None, :, :, None], grad_cs.shape)
    filt_grads = to_rows(rep_sum(jnp.concatenate([cross, skip_field], axis=1) * scale))
    conv_out = long_conv + skip_gain * mixed
    gated = (queries * conv_out).astype(jnp.bfloat16)
    out_terms = jnp.dot(gated, w_out, preferred_element_type=jnp.float32)
    layer_out = chan_reduce_scatter(out_terms).astype(jnp.bfloat16)
    grad_wout = lax.dot_general(
        gated, piece, (((0,), (0,)), ((), ())), preferred_element_type=jnp.float32
    )
    grad_queries = grad_gated * conv_out
    grad_mixed = back + skip_gain * grad_conv
    grad_pre = jnp.stack([grad_mixed * values, grad_mixed * keys, grad_queries]).astype(
        jnp.bfloat16
    )
    pre_blocks = grad_pre.reshape(3, row_count, block_count, BLOCK)
    d_input = jnp.einsum("smnj,nisj->mni", pre_blocks, w_blocks, preferred_element_type=jnp.float32)
    d_input = d_input.reshape(row_count, chan_width).astype(jnp.bfloat16)
    grad_win = jnp.einsum(
        "mni,smnj->nisj", input_blocks, pre_blocks, preferred_element_type=jnp.float32
    )
    grad_win = grad_win.reshape(chan_width, 3 * BLOCK) * scale
    grad_win, grad_wout = lax.psum((grad_win, grad_wout * scale), ("seq", "rep"))
    return (
        layer_out[None],
        d_input[None],
        grad_win,
        grad_wout,
        filt_grads[0],
        filt_grads[1],
        filt_grads[2, 0],
    )


def solution(mesh):
    return jax.shard_map(
        on_device,
        mesh=mesh,
        in_specs=(
            P("rep", "seq", "chan"),
            P("chan", None),
            P("chan", None),
            P("seq", "chan"),
            P("seq", "chan"),
            P("chan"),
            P("rep", "seq", "chan"),
        ),
        out_specs=(
            P("rep", "seq", "chan"),
            P("rep", "seq", "chan"),
            P("chan", None),
            P("chan", None),
            P("seq", "chan"),
            P("seq", "chan"),
            P("chan"),
        ),
        check_vma=False,
    )
```

```python
import math

import jax
import jax.numpy as jnp
import numpy as np
from jax import lax
from jax.sharding import PartitionSpec as P

BLOCK = 512

TABLE_PRECISION = lax.Precision.HIGH


def factor_split(length):
    second = 256
    return length // second, second


def unit_table(size):
    index_row = np.arange(size)
    angle = 2.0 * np.pi * ((index_row[:, None] * index_row[None, :]) % size) / size
    return (jnp.asarray(np.cos(angle), jnp.float32), jnp.asarray(np.sin(angle), jnp.float32))


def twiddle_table(rows, cols):
    length = rows * cols
    phase = (np.arange(rows)[:, None] * np.arange(cols)[None, :]) % length
    angle = 2.0 * np.pi * phase / length
    return (jnp.asarray(np.cos(angle), jnp.float32), jnp.asarray(np.sin(angle), jnp.float32))


def lead_apply(table, fields):
    return jnp.einsum("kn,nrm->krm", table, fields, precision=TABLE_PRECISION)


def minor_apply(fields, table):
    return jnp.einsum("krm,mj->krj", fields, table, precision=TABLE_PRECISION)


def real_spectrum(signal):
    first, field_count, width, second = signal.shape
    cos_a, sin_a = unit_table(first)
    cos_b, sin_b = unit_table(second)
    cos_t, sin_t = twiddle_table(first, second)
    grid = signal.reshape(first, field_count * width, second)
    y_re = lead_apply(cos_a, grid)
    y_im = lead_apply(-sin_a, grid)
    cos_t = cos_t[:, None, :]
    sin_t = sin_t[:, None, :]
    z_re = y_re * cos_t + y_im * sin_t
    z_im = y_im * cos_t - y_re * sin_t
    x_re = minor_apply(z_re, cos_b) + minor_apply(z_im, sin_b)
    x_im = minor_apply(z_im, cos_b) + minor_apply(z_re, -sin_b)
    return x_re.reshape(signal.shape), x_im.reshape(signal.shape)


def real_inverse(spec_re, spec_im):
    first, field_count, width, second = spec_re.shape
    length = first * second
    cos_a, sin_a = unit_table(first)
    cos_b, sin_b = unit_table(second)
    cos_t, sin_t = twiddle_table(first, second)
    flat_re = spec_re.reshape(first, field_count * width, second)
    flat_im = spec_im.reshape(first, field_count * width, second)
    a_re = minor_apply(flat_re, cos_b) + minor_apply(flat_im, -sin_b)
    a_im = minor_apply(flat_im, cos_b) + minor_apply(flat_re, sin_b)
    cos_t = cos_t[:, None, :] * (1.0 / length)
    sin_t = sin_t[:, None, :] * (1.0 / length)
    b_re = a_re * cos_t - a_im * sin_t
    b_im = a_re * sin_t + a_im * cos_t
    out = lead_apply(cos_a, b_re) + lead_apply(-sin_a, b_im)
    return out.reshape(spec_re.shape)


def complex_product(left_re, left_im, right_re, right_im):
    return (left_re * right_re - left_im * right_im, left_re * right_im + left_im * right_re)


def to_channels(fields):
    count = lax.axis_size("seq")
    field_count, rows, width = fields.shape
    parts = fields.reshape(field_count, rows, count, width // count).transpose(2, 0, 3, 1)
    return lax.all_to_all(parts, "seq", split_axis=0, concat_axis=0, tiled=True)


def to_rows(fields):
    count, field_count, width, rows = fields.shape
    gathered = lax.all_to_all(fields, "seq", split_axis=0, concat_axis=0, tiled=True)
    return gathered.transpose(1, 3, 0, 2).reshape(field_count, rows, count * width)


def rep_sum(value):
    count = lax.axis_size("rep")
    total = value
    for shift in range(1, count):
        pairs = [(i, (i + shift) % count) for i in range(count)]
        total = total + lax.ppermute(value, "rep", pairs)
    return total


def chan_reduce_scatter(terms):
    count = lax.axis_size("chan")
    rows, total_width = terms.shape
    pieces = terms.reshape(rows, count, total_width // count).transpose(1, 0, 2)
    received = lax.all_to_all(pieces, "chan", split_axis=0, concat_axis=0, tiled=True)
    total = received[0]
    for index in range(1, count):
        total = total + received[index]
    return total


def on_device(inputs, w_in, w_out, filt_fwd, filt_bwd, skip_gain, cotangent):
    input_rows = inputs[0]
    row_count, chan_width = input_rows.shape
    block_count = chan_width // BLOCK
    input_blocks = input_rows.reshape(row_count, block_count, BLOCK)
    w_blocks = w_in.reshape(block_count, BLOCK, 3, BLOCK)
    grad_rows = cotangent[0]
    chan_count = lax.axis_size("chan")
    copies = jnp.broadcast_to(grad_rows[None], (chan_count,) + grad_rows.shape)
    gathered = lax.all_to_all(copies, "chan", split_axis=0, concat_axis=0, tiled=True)
    piece = gathered.transpose(1, 0, 2).reshape(grad_rows.shape[0], -1)
    projected = jnp.einsum(
        "mni,nisj->smnj", input_blocks, w_blocks, preferred_element_type=jnp.float32
    )
    projected = projected.reshape(3, row_count, chan_width)
    keys, values, queries = (projected[0], projected[1], projected[2])
    mixed = keys * values
    grad_gated = lax.dot_general(
        piece, w_out, (((1,), (1,)), ((), ())), preferred_element_type=jnp.float32
    )
    grad_conv = grad_gated * queries
    spread = to_channels(jnp.stack([mixed, filt_fwd, filt_bwd, grad_conv]))
    spec_re, spec_im = real_spectrum(spread)
    mix_re, mix_im = (spec_re[:, 0], spec_im[:, 0])
    gain_re = spec_re[:, 1] + spec_re[:, 2]
    gain_im = spec_im[:, 1] - spec_im[:, 2]
    grad_re, grad_im = (spec_re[:, 3], spec_im[:, 3])
    joint_re, joint_im = complex_product(gain_re, gain_im, mix_re, mix_im)
    back_re, back_im = complex_product(gain_re, -gain_im, grad_re, grad_im)
    both = to_rows(
        real_inverse(
            jnp.stack([joint_re, back_re], axis=1), jnp.stack([joint_im, back_im], axis=1)
        )
    )
    long_conv = both[0]
    back = both[1]
    cross_re, cross_im = complex_product(grad_re, grad_im, mix_re, -mix_im)
    cross = real_inverse(
        jnp.stack([cross_re, cross_re], axis=1), jnp.stack([cross_im, -cross_im], axis=1)
    )
    scale = 1.0 / math.sqrt(lax.axis_size("rep") * lax.axis_size("seq") * row_count)
    filt_grads = to_rows(rep_sum(cross * scale))
    conv_out = long_conv + skip_gain * mixed
    gated = (queries * conv_out).astype(jnp.bfloat16)
    out_terms = jnp.dot(gated, w_out, preferred_element_type=jnp.float32)
    layer_out = chan_reduce_scatter(out_terms).astype(jnp.bfloat16)
    grad_wout = lax.dot_general(
        gated, piece, (((0,), (0,)), ((), ())), preferred_element_type=jnp.float32
    )
    grad_queries = grad_gated * conv_out
    grad_mixed = back + skip_gain * grad_conv
    grad_pre = jnp.stack([grad_mixed * values, grad_mixed * keys, grad_queries]).astype(
        jnp.bfloat16
    )
    pre_blocks = grad_pre.reshape(3, row_count, block_count, BLOCK)
    d_input = jnp.einsum("smnj,nisj->mni", pre_blocks, w_blocks, preferred_element_type=jnp.float32)
    d_input = d_input.reshape(row_count, chan_width).astype(jnp.bfloat16)
    grad_win = jnp.einsum(
        "mni,smnj->nisj", input_blocks, pre_blocks, preferred_element_type=jnp.float32
    )
    grad_win = grad_win.reshape(chan_width, 3 * BLOCK) * scale
    grad_skip = jnp.sum(grad_conv * mixed, axis=0)
    out_width = grad_wout.shape[1]
    skip_row = jnp.pad(grad_skip, (0, out_width - chan_width))[None]
    joined = jnp.concatenate([grad_wout, skip_row], axis=0) * scale
    grad_win, joined = lax.psum((grad_win, joined), ("seq", "rep"))
    return (
        layer_out[None],
        d_input[None],
        grad_win,
        joined[:chan_width],
        filt_grads[0],
        filt_grads[1],
        joined[chan_width, :chan_width],
    )


def solution(mesh):
    return jax.shard_map(
        on_device,
        mesh=mesh,
        in_specs=(
            P("rep", "seq", "chan"),
            P("chan", None),
            P("chan", None),
            P("seq", "chan"),
            P("seq", "chan"),
            P("chan"),
            P("rep", "seq", "chan"),
        ),
        out_specs=(
            P("rep", "seq", "chan"),
            P("rep", "seq", "chan"),
            P("chan", None),
            P("chan", None),
            P("seq", "chan"),
            P("seq", "chan"),
            P("chan"),
        ),
        check_vma=False,
    )
```

```python
import math

import jax
import jax.numpy as jnp
import numpy as np
from jax import lax
from jax.sharding import PartitionSpec as P

BLOCK = 512

TABLE_PRECISION = lax.Precision.HIGH


def factor_split(length):
    second = 256
    return length // second, second


def unit_table(size):
    index_row = np.arange(size)
    angle = 2.0 * np.pi * ((index_row[:, None] * index_row[None, :]) % size) / size
    return (jnp.asarray(np.cos(angle), jnp.float32), jnp.asarray(np.sin(angle), jnp.float32))


def twiddle_table(rows, cols):
    length = rows * cols
    phase = (np.arange(rows)[:, None] * np.arange(cols)[None, :]) % length
    angle = 2.0 * np.pi * phase / length
    return (jnp.asarray(np.cos(angle), jnp.float32), jnp.asarray(np.sin(angle), jnp.float32))


def lead_apply(table, fields):
    return jnp.einsum("kn,nrm->krm", table, fields, precision=TABLE_PRECISION)


def minor_apply(fields, table):
    return jnp.einsum("krm,mj->krj", fields, table, precision=TABLE_PRECISION)


def real_spectrum(signal):
    first, field_count, width, second = signal.shape
    cos_a, sin_a = unit_table(first)
    cos_b, sin_b = unit_table(second)
    cos_t, sin_t = twiddle_table(first, second)
    grid = signal.reshape(first, field_count * width, second)
    y_re = lead_apply(cos_a, grid)
    y_im = lead_apply(-sin_a, grid)
    cos_t = cos_t[:, None, :]
    sin_t = sin_t[:, None, :]
    z_re = y_re * cos_t + y_im * sin_t
    z_im = y_im * cos_t - y_re * sin_t
    x_re = minor_apply(z_re, cos_b) + minor_apply(z_im, sin_b)
    x_im = minor_apply(z_im, cos_b) + minor_apply(z_re, -sin_b)
    return x_re.reshape(signal.shape), x_im.reshape(signal.shape)


def real_inverse(spec_re, spec_im):
    first, field_count, width, second = spec_re.shape
    length = first * second
    cos_a, sin_a = unit_table(first)
    cos_b, sin_b = unit_table(second)
    cos_t, sin_t = twiddle_table(first, second)
    flat_re = spec_re.reshape(first, field_count * width, second)
    flat_im = spec_im.reshape(first, field_count * width, second)
    a_re = minor_apply(flat_re, cos_b) + minor_apply(flat_im, -sin_b)
    a_im = minor_apply(flat_im, cos_b) + minor_apply(flat_re, sin_b)
    cos_t = cos_t[:, None, :] * (1.0 / length)
    sin_t = sin_t[:, None, :] * (1.0 / length)
    b_re = a_re * cos_t - a_im * sin_t
    b_im = a_re * sin_t + a_im * cos_t
    out = lead_apply(cos_a, b_re) + lead_apply(-sin_a, b_im)
    return out.reshape(spec_re.shape)


def complex_product(left_re, left_im, right_re, right_im):
    return (left_re * right_re - left_im * right_im, left_re * right_im + left_im * right_re)


def to_channels(fields):
    count = lax.axis_size("seq")
    field_count, rows, width = fields.shape
    parts = fields.reshape(field_count, rows, count, width // count).transpose(2, 0, 3, 1)
    return lax.all_to_all(parts, "seq", split_axis=0, concat_axis=0, tiled=True)


def to_rows(fields):
    count, field_count, width, rows = fields.shape
    gathered = lax.all_to_all(fields, "seq", split_axis=0, concat_axis=0, tiled=True)
    return gathered.transpose(1, 3, 0, 2).reshape(field_count, rows, count * width)


def rep_sum(value):
    count = lax.axis_size("rep")
    total = value
    for shift in range(1, count):
        pairs = [(i, (i + shift) % count) for i in range(count)]
        total = total + lax.ppermute(value, "rep", pairs)
    return total


def chan_reduce_scatter(terms):
    count = lax.axis_size("chan")
    rows, total_width = terms.shape
    pieces = terms.reshape(rows, count, total_width // count).transpose(1, 0, 2)
    received = lax.all_to_all(pieces, "chan", split_axis=0, concat_axis=0, tiled=True)
    total = received[0]
    for index in range(1, count):
        total = total + received[index]
    return total


def on_device(inputs, w_in, w_out, filt_fwd, filt_bwd, skip_gain, cotangent):
    input_rows = inputs[0]
    row_count, chan_width = input_rows.shape
    block_count = chan_width // BLOCK
    input_blocks = input_rows.reshape(row_count, block_count, BLOCK)
    w_blocks = w_in.reshape(block_count, BLOCK, 3, BLOCK)
    grad_rows = cotangent[0]
    chan_count = lax.axis_size("chan")
    shifted = [grad_rows]
    for shift in range(1, chan_count):
        pairs = [(i, (i + shift) % chan_count) for i in range(chan_count)]
        shifted.append(lax.ppermute(grad_rows, "chan", pairs))
    chan_index = lax.axis_index("chan")
    order = (chan_index - jnp.arange(chan_count, dtype=jnp.int32)) % chan_count
    gathered = jnp.take(jnp.stack(shifted), order, axis=0)
    piece = gathered.transpose(1, 0, 2).reshape(grad_rows.shape[0], -1)
    projected = jnp.einsum(
        "mni,nisj->smnj", input_blocks, w_blocks, preferred_element_type=jnp.float32
    )
    projected = projected.reshape(3, row_count, chan_width)
    keys, values, queries = (projected[0], projected[1], projected[2])
    mixed = keys * values
    grad_gated = lax.dot_general(
        piece, w_out, (((1,), (1,)), ((), ())), preferred_element_type=jnp.float32
    )
    grad_conv = grad_gated * queries
    spec_re, spec_im = real_spectrum(to_channels(jnp.stack([mixed, filt_fwd, filt_bwd])))
    mix_re, mix_im = (spec_re[:, 0], spec_im[:, 0])
    gain_re = spec_re[:, 1] + spec_re[:, 2]
    gain_im = spec_im[:, 1] - spec_im[:, 2]
    grad_re, grad_im = real_spectrum(to_channels(grad_conv[None]))
    grad_re, grad_im = (grad_re[:, 0], grad_im[:, 0])
    joint_re, joint_im = complex_product(gain_re, gain_im, mix_re, mix_im)
    back_re, back_im = complex_product(gain_re, -gain_im, grad_re, grad_im)
    both = to_rows(
        real_inverse(
            jnp.stack([joint_re, back_re], axis=1), jnp.stack([joint_im, back_im], axis=1)
        )
    )
    long_conv = both[0]
    back = both[1]
    cross_re, cross_im = complex_product(grad_re, grad_im, mix_re, -mix_im)
    cross = real_inverse(
        jnp.stack([cross_re, cross_re], axis=1), jnp.stack([cross_im, -cross_im], axis=1)
    )
    scale = 1.0 / math.sqrt(lax.axis_size("rep") * lax.axis_size("seq") * row_count)
    filt_grads = to_rows(rep_sum(cross * scale))
    conv_out = long_conv + skip_gain * mixed
    gated = (queries * conv_out).astype(jnp.bfloat16)
    out_terms = jnp.dot(gated, w_out, preferred_element_type=jnp.float32)
    layer_out = chan_reduce_scatter(out_terms).astype(jnp.bfloat16)
    grad_wout = lax.dot_general(
        gated, piece, (((0,), (0,)), ((), ())), preferred_element_type=jnp.float32
    )
    grad_queries = grad_gated * conv_out
    grad_mixed = back + skip_gain * grad_conv
    grad_pre = jnp.stack([grad_mixed * values, grad_mixed * keys, grad_queries]).astype(
        jnp.bfloat16
    )
    pre_blocks = grad_pre.reshape(3, row_count, block_count, BLOCK)
    d_input = jnp.einsum("smnj,nisj->mni", pre_blocks, w_blocks, preferred_element_type=jnp.float32)
    d_input = d_input.reshape(row_count, chan_width).astype(jnp.bfloat16)
    grad_win = jnp.einsum(
        "mni,smnj->nisj", input_blocks, pre_blocks, preferred_element_type=jnp.float32
    )
    grad_win = grad_win.reshape(chan_width, 3 * BLOCK) * scale
    grad_skip = jnp.sum(grad_conv * mixed, axis=0)
    out_width = grad_wout.shape[1]
    skip_row = jnp.pad(grad_skip, (0, out_width - chan_width))[None]
    joined = jnp.concatenate([grad_wout, skip_row], axis=0) * scale
    grad_win, joined = lax.psum((grad_win, joined), ("seq", "rep"))
    return (
        layer_out[None],
        d_input[None],
        grad_win,
        joined[:chan_width],
        filt_grads[0],
        filt_grads[1],
        joined[chan_width, :chan_width],
    )


def solution(mesh):
    return jax.shard_map(
        on_device,
        mesh=mesh,
        in_specs=(
            P("rep", "seq", "chan"),
            P("chan", None),
            P("chan", None),
            P("seq", "chan"),
            P("seq", "chan"),
            P("chan"),
            P("rep", "seq", "chan"),
        ),
        out_specs=(
            P("rep", "seq", "chan"),
            P("rep", "seq", "chan"),
            P("chan", None),
            P("chan", None),
            P("seq", "chan"),
            P("seq", "chan"),
            P("chan"),
        ),
        check_vma=False,
    )
```

```python
import math

import jax
import jax.numpy as jnp
import numpy as np
from jax import lax
from jax.sharding import PartitionSpec as P

BLOCK = 512

TABLE_PRECISION = lax.Precision.HIGH


def factor_split(length):
    second = 256
    return length // second, second


def unit_table(size):
    index_row = np.arange(size)
    angle = 2.0 * np.pi * ((index_row[:, None] * index_row[None, :]) % size) / size
    return (jnp.asarray(np.cos(angle), jnp.float32), jnp.asarray(np.sin(angle), jnp.float32))


def twiddle_table(rows, cols):
    length = rows * cols
    phase = (np.arange(rows)[:, None] * np.arange(cols)[None, :]) % length
    angle = 2.0 * np.pi * phase / length
    return (jnp.asarray(np.cos(angle), jnp.float32), jnp.asarray(np.sin(angle), jnp.float32))


def lead_apply(table, fields):
    return jnp.einsum("kn,nrm->krm", table, fields, precision=TABLE_PRECISION)


def minor_apply(fields, table):
    return jnp.einsum("krm,mj->krj", fields, table, precision=TABLE_PRECISION)


def real_spectrum(signal):
    first, field_count, width, second = signal.shape
    cos_a, sin_a = unit_table(first)
    cos_b, sin_b = unit_table(second)
    cos_t, sin_t = twiddle_table(first, second)
    grid = signal.reshape(first, field_count * width, second)
    y = lead_apply(jnp.concatenate([cos_a, -sin_a], axis=0), grid)
    y_re, y_im = (y[:first], y[first:])
    cos_t = cos_t[:, None, :]
    sin_t = sin_t[:, None, :]
    z = jnp.concatenate([y_re * cos_t + y_im * sin_t, y_im * cos_t - y_re * sin_t], axis=2)
    table = jnp.concatenate(
        [jnp.concatenate([cos_b, -sin_b], axis=1), jnp.concatenate([sin_b, cos_b], axis=1)], axis=0
    )
    x = minor_apply(z, table)
    return x[..., :second].reshape(signal.shape), x[..., second:].reshape(signal.shape)


def real_inverse(spec_re, spec_im):
    first, field_count, width, second = spec_re.shape
    length = first * second
    cos_a, sin_a = unit_table(first)
    cos_b, sin_b = unit_table(second)
    cos_t, sin_t = twiddle_table(first, second)
    flat = jnp.concatenate(
        [
            spec_re.reshape(first, field_count * width, second),
            spec_im.reshape(first, field_count * width, second),
        ],
        axis=2,
    )
    table = jnp.concatenate(
        [jnp.concatenate([cos_b, sin_b], axis=1), jnp.concatenate([-sin_b, cos_b], axis=1)], axis=0
    )
    a = minor_apply(flat, table)
    a_re, a_im = (a[..., :second], a[..., second:])
    cos_t = cos_t[:, None, :] * (1.0 / length)
    sin_t = sin_t[:, None, :] * (1.0 / length)
    b = jnp.concatenate([a_re * cos_t - a_im * sin_t, a_re * sin_t + a_im * cos_t], axis=0)
    out = lead_apply(jnp.concatenate([cos_a, -sin_a], axis=1), b)
    return out.reshape(spec_re.shape)


def complex_product(left_re, left_im, right_re, right_im):
    return (left_re * right_re - left_im * right_im, left_re * right_im + left_im * right_re)


def to_channels(fields):
    count = lax.axis_size("seq")
    field_count, rows, width = fields.shape
    parts = fields.reshape(field_count, rows, count, width // count).transpose(2, 0, 3, 1)
    return lax.all_to_all(parts, "seq", split_axis=0, concat_axis=0, tiled=True)


def to_rows(fields):
    count, field_count, width, rows = fields.shape
    gathered = lax.all_to_all(fields, "seq", split_axis=0, concat_axis=0, tiled=True)
    return gathered.transpose(1, 3, 0, 2).reshape(field_count, rows, count * width)


def rep_sum(value):
    count = lax.axis_size("rep")
    total = value
    for shift in range(1, count):
        pairs = [(i, (i + shift) % count) for i in range(count)]
        total = total + lax.ppermute(value, "rep", pairs)
    return total


def chan_reduce_scatter(terms):
    count = lax.axis_size("chan")
    rows, total_width = terms.shape
    pieces = terms.reshape(rows, count, total_width // count).transpose(1, 0, 2)
    received = lax.all_to_all(pieces, "chan", split_axis=0, concat_axis=0, tiled=True)
    total = received[0]
    for index in range(1, count):
        total = total + received[index]
    return total


def on_device(inputs, w_in, w_out, filt_fwd, filt_bwd, skip_gain, cotangent):
    input_rows = inputs[0]
    row_count, chan_width = input_rows.shape
    block_count = chan_width // BLOCK
    input_blocks = input_rows.reshape(row_count, block_count, BLOCK)
    w_blocks = w_in.reshape(block_count, BLOCK, 3, BLOCK)
    grad_rows = cotangent[0]
    chan_count = lax.axis_size("chan")
    copies = jnp.broadcast_to(grad_rows[None], (chan_count,) + grad_rows.shape)
    gathered = lax.all_to_all(copies, "chan", split_axis=0, concat_axis=0, tiled=True)
    piece = gathered.transpose(1, 0, 2).reshape(grad_rows.shape[0], -1)
    projected = jnp.einsum(
        "mni,nisj->smnj", input_blocks, w_blocks, preferred_element_type=jnp.float32
    )
    projected = projected.reshape(3, row_count, chan_width)
    keys, values, queries = (projected[0], projected[1], projected[2])
    mixed = keys * values
    grad_gated = lax.dot_general(
        piece, w_out, (((1,), (1,)), ((), ())), preferred_element_type=jnp.float32
    )
    grad_conv = grad_gated * queries
    spread = to_channels(jnp.stack([mixed, filt_fwd, filt_bwd, grad_conv]))
    spec_re, spec_im = real_spectrum(spread)
    mix_re, mix_im = (spec_re[:, 0], spec_im[:, 0])
    gain_re = spec_re[:, 1] + spec_re[:, 2]
    gain_im = spec_im[:, 1] - spec_im[:, 2]
    grad_re, grad_im = (spec_re[:, 3], spec_im[:, 3])
    joint_re, joint_im = complex_product(gain_re, gain_im, mix_re, mix_im)
    back_re, back_im = complex_product(gain_re, -gain_im, grad_re, grad_im)
    both = to_rows(
        real_inverse(
            jnp.stack([joint_re, back_re], axis=1), jnp.stack([joint_im, back_im], axis=1)
        )
    )
    long_conv = both[0]
    back = both[1]
    cross_re, cross_im = complex_product(grad_re, grad_im, mix_re, -mix_im)
    cross = real_inverse(
        jnp.stack([cross_re, cross_re], axis=1), jnp.stack([cross_im, -cross_im], axis=1)
    )
    scale = 1.0 / math.sqrt(lax.axis_size("rep") * lax.axis_size("seq") * row_count)
    filt_grads = to_rows(rep_sum(cross * scale))
    conv_out = long_conv + skip_gain * mixed
    gated = (queries * conv_out).astype(jnp.bfloat16)
    out_terms = jnp.dot(gated, w_out, preferred_element_type=jnp.float32)
    layer_out = chan_reduce_scatter(out_terms).astype(jnp.bfloat16)
    grad_wout = lax.dot_general(
        gated, piece, (((0,), (0,)), ((), ())), preferred_element_type=jnp.float32
    )
    grad_queries = grad_gated * conv_out
    grad_mixed = back + skip_gain * grad_conv
    grad_pre = jnp.stack([grad_mixed * values, grad_mixed * keys, grad_queries]).astype(
        jnp.bfloat16
    )
    pre_blocks = grad_pre.reshape(3, row_count, block_count, BLOCK)
    d_input = jnp.einsum("smnj,nisj->mni", pre_blocks, w_blocks, preferred_element_type=jnp.float32)
    d_input = d_input.reshape(row_count, chan_width).astype(jnp.bfloat16)
    grad_win = jnp.einsum(
        "mni,smnj->nisj", input_blocks, pre_blocks, preferred_element_type=jnp.float32
    )
    grad_win = grad_win.reshape(chan_width, 3 * BLOCK) * scale
    grad_skip = jnp.sum(grad_conv * mixed, axis=0)
    out_width = grad_wout.shape[1]
    skip_row = jnp.pad(grad_skip, (0, out_width - chan_width))[None]
    joined = jnp.concatenate([grad_wout, skip_row], axis=0) * scale
    grad_win, joined = lax.psum((grad_win, joined), ("seq", "rep"))
    return (
        layer_out[None],
        d_input[None],
        grad_win,
        joined[:chan_width],
        filt_grads[0],
        filt_grads[1],
        joined[chan_width, :chan_width],
    )


def solution(mesh):
    return jax.shard_map(
        on_device,
        mesh=mesh,
        in_specs=(
            P("rep", "seq", "chan"),
            P("chan", None),
            P("chan", None),
            P("seq", "chan"),
            P("seq", "chan"),
            P("chan"),
            P("rep", "seq", "chan"),
        ),
        out_specs=(
            P("rep", "seq", "chan"),
            P("rep", "seq", "chan"),
            P("chan", None),
            P("chan", None),
            P("seq", "chan"),
            P("seq", "chan"),
            P("chan"),
        ),
        check_vma=False,
    )
```
